512 devices in a mesh: blk: 64 (over y, x, z_hi, core), mp: 8 (over z_lo).
Axes of the slice: x: 4, y: 4, z: 16 (z_hi: 2, z_lo: 8; z = z_hi * 8 + z_lo), core: 2. Of those that a mesh axis runs over, the one named last changes fastest.
Arguments:
- queries: bfloat16 [16384, 5120], P('blk', 'mp'), may hold values from -8.5 to 8.5
- suffix_key_rows: bfloat16 [16384, 1024], P('blk', 'mp'), may hold values from -6 to 6
- suffix_value_rows: bfloat16 [16384, 1024], P('blk', 'mp'), may hold values from -6 to 6
- shared_prefix_keys: bfloat16 [2048, 1024], P('blk', 'mp'), may hold values from -8.5 to 8.5
- shared_prefix_values: bfloat16 [2048, 1024], P('blk', 'mp'), may hold values from -6 to 6
- out_weight: bfloat16 [5120, 5120], P('mp', 'blk'), may hold values from -0.078125 to 0.078125
- lengths: int32 [16], replicated, may hold values from 1 to 4096, 16384 in all
Outputs:
- output: bfloat16 [16384, 5120], P('blk', 'mp')
The draws below stay inside these ranges and needn't reach their ends.
Inputs may be any that keep to these rules, and one draw needn't show every extreme that they name: The lengths sum to 16384; the longest is exactly 4096.
All inputs are finite; a program needn't handle non-finite values.
Results may differ from the reference program's by a relative error of at most 0.019.
Values may be sent and summed in bfloat16 or wider, within the bound.
No kernel may reach another device: no remote copies, remote signals or barrier semaphores. Data moves between devices by JAX's collectives and lax.ppermute only.
A program may use at most 64 MiB of HBM per device.

```python
import math
import jax
import jax.numpy as jnp
import numpy as np
from jax import lax

D = 5120
QUERY_HEADS = 40
KEY_VALUE_HEADS = 8
HEAD_SIZE = 128
REQS = 16
SUF_DEV = 256
SUFFIX_TOKENS = 16384
PREFIX_TOKENS = 2048
LONGEST_SUFFIX = 4096
N_MP = 8


def pair_base(key):
    base_key = jax.random.fold_in(key, 11)
    key_query, prefix_key_slice = jax.random.split(base_key)
    query_base = jnp.clip(jax.random.normal(key_query, (SUFFIX_TOKENS, QUERY_HEADS * HEAD_SIZE), jnp.float32), -6.0, 6.0)
    prefix_start_index = jnp.clip(jax.random.normal(prefix_key_slice, (PREFIX_TOKENS, KEY_VALUE_HEADS * HEAD_SIZE), jnp.float32), -6.0, 6.0)
    return (query_base, prefix_start_index)


def draw_shared_prefix_keys(key, part):
    query_base, prefix_start_index = pair_base(key)
    return prefix_start_index.astype(jnp.bfloat16)


def draw_queries(key, part):
    query_base, prefix_start_index = pair_base(key)
    return query_base.astype(jnp.bfloat16)


def block_scale(own_key, shape, pieces, low, largest):
    def one(position, parts):
        draws = jax.random.uniform(jax.random.fold_in(jax.random.fold_in(own_key, 6), position), (parts,), jnp.float32, low / len(pieces), largest / len(pieces))
        return jnp.repeat(jnp.exp(draws), shape[position] // parts).reshape((-1,) + (1,) * (len(shape) - position - 1))

    factor_of = one(*pieces[0])
    for cut in pieces[1:]:
        factor_of = factor_of * one(*cut)
    return factor_of


def length_profile(amount, total, most, lean):
    loads = [(1 << 20) // math.isqrt(standing ** lean) + 1 for standing in range(2, amount + 1)]
    rest, counts = total - most - (amount - 1), [1] * (amount - 1)
    while rest > 0:
        movable = [i for i in range(amount - 1) if counts[i] < most]
        pool, budget = sum([loads[i] for i in movable]), rest
        for i in movable:
            more = min(most - counts[i], max(1, budget * loads[i] // pool), rest)
            counts[i] = counts[i] + more
            rest = rest - more
    return np.array([most] + counts)


def uneven(stream_key, amount, total, limit, slope):
    if amount == 2:
        one = jax.random.randint(stream_key, (), max(1, total - limit), min(limit, total - 1) + 1)
        return jnp.stack([one, total - one])
    sizes = jnp.asarray(length_profile(amount, total, limit, slope), jnp.int32)
    twos = (amount - 1) // 2
    donor, sink = sizes[1:1 + 2 * twos:2], sizes[2:2 + 2 * twos:2]
    room = jnp.minimum(donor - 1, limit - sink)
    shifted = jax.random.randint(jax.random.fold_in(stream_key, 1), (twos,), 0, 1 << 20) % (room + 1)
    sizes = sizes.at[1:1 + 2 * twos:2].set(donor - shifted).at[2:2 + 2 * twos:2].set(sink + shifted)
    return sizes[jax.random.permutation(jax.random.fold_in(stream_key, 2), amount)]


def gaussian(rng, extent, deviation, reach, cuts=(), held_as=jnp.bfloat16):
    drawn = jax.random.normal(rng, extent, jnp.float32) * deviation
    if len(cuts) > 0:
        drawn = block_scale(rng, extent, cuts, -0.22, 0.18) * drawn
    return jnp.clip(drawn, min=-reach, max=reach).astype(held_as)


def setup_inputs(seed: int = 0) -> dict:
    arg_keys = jax.random.split(jax.random.key(seed), 8)
    queries = draw_queries(jax.random.fold_in(arg_keys[7], 71), 0)
    suffix_key_rows = gaussian(arg_keys[1], (SUFFIX_TOKENS, KEY_VALUE_HEADS * HEAD_SIZE), 1.0, 6.0, ((0, 64), (1, 8)))
    suffix_value_rows = gaussian(arg_keys[2], (SUFFIX_TOKENS, KEY_VALUE_HEADS * HEAD_SIZE), 1.0, 6.0, ((0, 64), (1, 8)))
    shared_prefix_keys = draw_shared_prefix_keys(jax.random.fold_in(arg_keys[7], 71), 0)
    shared_prefix_values = gaussian(arg_keys[4], (PREFIX_TOKENS, KEY_VALUE_HEADS * HEAD_SIZE), 1.0, 6.0, ((0, 64), (1, 8)))
    out_weight = gaussian(arg_keys[5], (QUERY_HEADS * HEAD_SIZE, D), (QUERY_HEADS * HEAD_SIZE) ** -0.5, 0.078125, ((0, 8), (1, 64)))
    lengths = uneven(arg_keys[6], REQS, SUFFIX_TOKENS, LONGEST_SUFFIX, 2).astype(jnp.int32)
    return {"queries": queries, "suffix_key_rows": suffix_key_rows, "suffix_value_rows": suffix_value_rows, "shared_prefix_keys": shared_prefix_keys, "shared_prefix_values": shared_prefix_values, "out_weight": out_weight, "lengths": lengths}


MASKED_SCORE = -1e+30

def reference(queries, suffix_key_rows, suffix_value_rows, shared_prefix_keys, shared_prefix_values, out_weight, lengths):
    heads_per_group = QUERY_HEADS // KEY_VALUE_HEADS
    score_scale = 1.0 / math.sqrt(HEAD_SIZE)
    req_ends = jnp.cumsum(lengths).astype(jnp.int32)
    positions = jnp.arange(SUFFIX_TOKENS, dtype=jnp.int32)
    owners = lax.optimization_barrier(jnp.sum((positions[:, None] >= req_ends[None, :]).astype(jnp.int32), axis=1)).astype(jnp.int32)
    rows_per_block = SUF_DEV
    visible_window = LONGEST_SUFFIX + rows_per_block
    padded_keys = jnp.concatenate([jnp.zeros((LONGEST_SUFFIX, KEY_VALUE_HEADS * HEAD_SIZE), jnp.bfloat16), suffix_key_rows], axis=0)
    padded_values = jnp.concatenate([jnp.zeros((LONGEST_SUFFIX, KEY_VALUE_HEADS * HEAD_SIZE), jnp.bfloat16), suffix_value_rows], axis=0)
    pad_owners = jnp.concatenate([jnp.full((LONGEST_SUFFIX,), -1, jnp.int32), owners], axis=0)
    prefix_key_rows = shared_prefix_keys.astype(jnp.float32).reshape(PREFIX_TOKENS, KEY_VALUE_HEADS, HEAD_SIZE)
    prefix_value_rows = shared_prefix_values.astype(jnp.float32).reshape(PREFIX_TOKENS, KEY_VALUE_HEADS, HEAD_SIZE)

    def one_block(start_index):
        start_index = start_index.astype(jnp.int32)
        query_row_slice = lax.dynamic_slice_in_dim(queries, start_index, rows_per_block, 0)
        heads_of_query = query_row_slice.astype(jnp.float32).reshape(rows_per_block, KEY_VALUE_HEADS, heads_per_group, HEAD_SIZE)
        key_row_slice = lax.dynamic_slice_in_dim(padded_keys, start_index, visible_window, 0).astype(jnp.float32).reshape(visible_window, KEY_VALUE_HEADS, HEAD_SIZE)
        value_row_slice = lax.dynamic_slice_in_dim(padded_values, start_index, visible_window, 0).astype(jnp.float32).reshape(visible_window, KEY_VALUE_HEADS, HEAD_SIZE)
        key_owner = lax.dynamic_slice_in_dim(pad_owners, start_index, visible_window, 0)
        query_owner = lax.dynamic_slice_in_dim(owners, start_index, rows_per_block, 0)
        key_pos = start_index - LONGEST_SUFFIX + jnp.arange(visible_window, dtype=jnp.int32)
        query_pos = start_index + jnp.arange(rows_per_block, dtype=jnp.int32)
        visible = (key_owner[None, :] == query_owner[:, None]) & (key_pos[None, :] <= query_pos[:, None]) & (key_pos[None, :] >= 0)
        pre_scores = jnp.einsum('qhgd,khd->hgqk', heads_of_query, prefix_key_rows) * score_scale
        suf_scores = jnp.einsum('qhgd,khd->hgqk', heads_of_query, key_row_slice) * score_scale
        suf_scores = jnp.where(visible[None, None], suf_scores, MASKED_SCORE)
        peak = jnp.maximum(lax.optimization_barrier(jnp.max(pre_scores, axis=-1)), lax.optimization_barrier(jnp.max(suf_scores, axis=-1)))
        pre_weights = jnp.exp(pre_scores - peak[..., None])
        suf_weights = jnp.where(visible[None, None], jnp.exp(suf_scores - peak[..., None]), 0.0)
        total = lax.optimization_barrier(jnp.sum(pre_weights, axis=-1)) + lax.optimization_barrier(jnp.sum(suf_weights, axis=-1))
        pre_low = lax.optimization_barrier(pre_weights.astype(jnp.bfloat16)).astype(jnp.float32)
        suf_low = lax.optimization_barrier(suf_weights.astype(jnp.bfloat16)).astype(jnp.float32)
        summed = jnp.einsum('hgqk,khd->hgqd', pre_low, prefix_value_rows) + jnp.einsum('hgqk,khd->hgqd', suf_low, value_row_slice)
        attended = summed / total[..., None]
        return jnp.transpose(attended, (2, 0, 1, 3)).reshape(rows_per_block, QUERY_HEADS * HEAD_SIZE).astype(jnp.bfloat16)
    starts = jnp.arange(SUFFIX_TOKENS // rows_per_block, dtype=jnp.int32) * rows_per_block
    attn = lax.map(one_block, starts).reshape(SUFFIX_TOKENS, QUERY_HEADS * HEAD_SIZE)
    group_cols = QUERY_HEADS * HEAD_SIZE // N_MP
    summed_out = jnp.zeros((SUFFIX_TOKENS, D), jnp.float32)
    for group_index in range(N_MP):
        attn_cols = attn[:, group_index * group_cols:(group_index + 1) * group_cols]
        weight_rows = out_weight[group_index * group_cols:(group_index + 1) * group_cols]
        partial_value = jnp.dot(attn_cols, weight_rows, preferred_element_type=jnp.float32)
        partial_value = lax.optimization_barrier(partial_value.astype(jnp.bfloat16)).astype(jnp.float32)
        summed_out = summed_out + partial_value
    return summed_out.astype(jnp.bfloat16)
```

```python
import math

import jax
import jax.numpy as jnp
from jax import lax
from jax.sharding import PartitionSpec as P

HEAD_SIZE = 128


MASKED_SCORE = -1e30


def shifted(block, axis, distance):
    devices = lax.axis_size(axis)
    route = [((i - distance) % devices, i) for i in range(devices)]
    return lax.ppermute(block, axis, route)


def shifted_pair(first, second, axis, distance):
    rows = first.shape[0] * first.shape[1]
    packed = jnp.concatenate(
        (first.reshape(rows, first.shape[2]), second.reshape(-1, second.shape[2])), axis=0
    )
    packed = shifted(packed, axis, distance)
    return (
        packed[:rows].reshape(first.shape),
        packed[rows:].reshape(second.shape),
    )


def per_device(
    queries,
    suffix_key_rows,
    suffix_value_rows,
    shared_prefix_keys,
    shared_prefix_values,
    out_weight,
    lengths,
):
    tok_rows = queries.shape[0]
    kv_heads = suffix_key_rows.shape[1] // HEAD_SIZE
    q_heads = queries.shape[1] // HEAD_SIZE
    heads_per_group = q_heads // kv_heads
    blocks = lax.axis_size("blk")
    my_block = lax.axis_index("blk")
    score_scale = 1.0 / math.sqrt(HEAD_SIZE)
    width = kv_heads * HEAD_SIZE

    own_kv = jnp.concatenate((suffix_key_rows, suffix_value_rows), axis=1)[None]
    prefix = jnp.concatenate((shared_prefix_keys, shared_prefix_values), axis=1)[None]
    suffix = own_kv
    distance = 1
    while 2 * distance <= blocks // 4:
        got_suffix, got_prefix = shifted_pair(suffix, prefix, "blk", distance)
        suffix = jnp.concatenate((got_suffix, suffix), axis=0)
        prefix = jnp.concatenate((got_prefix, prefix), axis=0)
        distance *= 2
    got_suffix, got_prefix = shifted_pair(own_kv, prefix, "blk", distance)
    suffix = jnp.concatenate((got_suffix, suffix), axis=0)
    prefix = jnp.concatenate((got_prefix, prefix), axis=0)
    distance *= 2
    while distance < blocks:
        prefix = jnp.concatenate((shifted(prefix, "blk", distance), prefix), axis=0)
        distance *= 2

    reach = suffix.shape[0]
    suffix = suffix.reshape(reach * tok_rows, 2 * width)
    prefix = prefix.reshape(-1, 2 * width)

    req_ends = jnp.cumsum(lengths)
    local_rows = jnp.arange(tok_rows, dtype=jnp.int32)
    query_pos = my_block * tok_rows + local_rows

    def owner_of(position):
        return jnp.sum((position[:, None] >= req_ends[None, :]).astype(jnp.int32), axis=1)

    query_owner = owner_of(query_pos)
    key_pos = (my_block - (reach - 1)) * tok_rows + jnp.arange(reach * tok_rows, dtype=jnp.int32)
    key_owner = owner_of(key_pos)
    visible = (
        (key_owner[None, :] == query_owner[:, None])
        & (key_pos[None, :] <= query_pos[:, None])
        & (key_pos[None, :] >= 0)
    )

    heads_of_query = queries.reshape(tok_rows, kv_heads, heads_per_group, HEAD_SIZE)

    def one_head(kv_head):
        cols = slice(kv_head * HEAD_SIZE, (kv_head + 1) * HEAD_SIZE)
        vcols = slice(width + kv_head * HEAD_SIZE, width + (kv_head + 1) * HEAD_SIZE)
        q = heads_of_query[:, kv_head]
        pre_scores = (
            jnp.einsum("qgd,kd->gqk", q, prefix[:, cols], preferred_element_type=jnp.float32)
            * score_scale
        )
        suf_scores = (
            jnp.einsum("qgd,kd->gqk", q, suffix[:, cols], preferred_element_type=jnp.float32)
            * score_scale
        )
        suf_scores = jnp.where(visible[None], suf_scores, MASKED_SCORE)
        peak = jnp.maximum(jnp.max(pre_scores, axis=-1), jnp.max(suf_scores, axis=-1))
        pre_weights = jnp.exp(pre_scores - peak[..., None])
        suf_weights = jnp.where(visible[None], jnp.exp(suf_scores - peak[..., None]), 0.0)
        total = jnp.sum(pre_weights, axis=-1) + jnp.sum(suf_weights, axis=-1)
        summed = jnp.einsum(
            "gqk,kd->gqd",
            pre_weights.astype(jnp.bfloat16),
            prefix[:, vcols],
            preferred_element_type=jnp.float32,
        ) + jnp.einsum(
            "gqk,kd->gqd",
            suf_weights.astype(jnp.bfloat16),
            suffix[:, vcols],
            preferred_element_type=jnp.float32,
        )
        return summed / total[..., None]

    attended = jnp.stack([one_head(h) for h in range(kv_heads)])
    attn = (
        jnp.transpose(attended, (2, 0, 1, 3))
        .reshape(tok_rows, q_heads * HEAD_SIZE)
        .astype(jnp.bfloat16)
    )
    product = jnp.dot(
        attn,
        lax.all_gather(out_weight, "blk", axis=1, tiled=True),
        preferred_element_type=jnp.float32,
    )
    return lax.psum_scatter(product.astype(jnp.bfloat16), "mp", scatter_dimension=1, tiled=True)


def solution(mesh):
    placed = (
        P("blk", "mp"),
        P("blk", "mp"),
        P("blk", "mp"),
        P("blk", "mp"),
        P("blk", "mp"),
        P("mp", "blk"),
        P(),
    )
    return jax.shard_map(
        per_device, mesh=mesh, in_specs=placed, out_specs=P("blk", "mp"), check_vma=False
    )
```

```python
import math

import jax
import jax.numpy as jnp
from jax import lax
from jax.sharding import PartitionSpec as P

HEAD_SIZE = 128


MASKED_SCORE = -1e30


BLK_PARTS = (("y", 4), ("x", 4), ("zh", 2), ("core", 2))
BLK = tuple(name for name, _ in BLK_PARTS)
BLOCKS = math.prod(size for _, size in BLK_PARTS)


def shifted(block, axis, distance):
    devices = BLOCKS
    route = [((i - distance) % devices, i) for i in range(devices)]
    return lax.ppermute(block, axis, route)


def shifted_pair(first, second, axis, distance):
    rows = first.shape[0] * first.shape[1]
    packed = jnp.concatenate(
        (first.reshape(rows, first.shape[2]), second.reshape(-1, second.shape[2])), axis=0
    )
    packed = shifted(packed, axis, distance)
    return (
        packed[:rows].reshape(first.shape),
        packed[rows:].reshape(second.shape),
    )


def per_device(
    queries,
    suffix_key_rows,
    suffix_value_rows,
    shared_prefix_keys,
    shared_prefix_values,
    out_weight,
    lengths,
):
    tok_rows = queries.shape[0]
    kv_heads = suffix_key_rows.shape[1] // HEAD_SIZE
    q_heads = queries.shape[1] // HEAD_SIZE
    heads_per_group = q_heads // kv_heads
    blocks = BLOCKS
    my_block = lax.axis_index(BLK)
    score_scale = 1.0 / math.sqrt(HEAD_SIZE)
    width = kv_heads * HEAD_SIZE

    own_kv = jnp.concatenate((suffix_key_rows, suffix_value_rows), axis=1)[None]
    prefix = jnp.concatenate((shared_prefix_keys, shared_prefix_values), axis=1)[None]
    suffix = own_kv
    reach = blocks // 4
    shifts = [1 << k for k in range(reach.bit_length() - 1)]
    shifts = shifts[1:2] + shifts[:1] + shifts[2:][::-1]
    distances = [0]
    for distance in shifts:
        got_suffix, got_prefix = shifted_pair(suffix, prefix, BLK, distance)
        suffix = jnp.concatenate((got_suffix, suffix), axis=0)
        prefix = jnp.concatenate((got_prefix, prefix), axis=0)
        distances = [d + distance for d in distances] + distances
    got_suffix, got_prefix = shifted_pair(own_kv, prefix, BLK, reach)
    suffix = jnp.concatenate((got_suffix, suffix), axis=0)
    prefix = jnp.concatenate((got_prefix, prefix), axis=0)
    distances = [reach] + distances
    distance = 2 * reach
    while distance < blocks:
        prefix = jnp.concatenate((shifted(prefix, BLK, distance), prefix), axis=0)
        distance *= 2

    count = suffix.shape[0]
    suffix = suffix.reshape(count * tok_rows, 2 * width)
    prefix = prefix.reshape(-1, 2 * width)

    req_ends = jnp.cumsum(lengths)
    local_rows = jnp.arange(tok_rows, dtype=jnp.int32)
    query_pos = my_block * tok_rows + local_rows

    def owner_of(position):
        return jnp.sum((position[:, None] >= req_ends[None, :]).astype(jnp.int32), axis=1)

    query_owner = owner_of(query_pos)
    block_of_key = my_block - jnp.repeat(jnp.array(distances, jnp.int32), tok_rows)
    key_pos = block_of_key * tok_rows + jnp.tile(local_rows, count)
    key_owner = owner_of(key_pos)
    visible = (
        (key_owner[None, :] == query_owner[:, None])
        & (key_pos[None, :] <= query_pos[:, None])
        & (key_pos[None, :] >= 0)
    )

    heads_of_query = queries.reshape(tok_rows, kv_heads, heads_per_group, HEAD_SIZE)

    def one_head(kv_head):
        cols = slice(kv_head * HEAD_SIZE, (kv_head + 1) * HEAD_SIZE)
        vcols = slice(width + kv_head * HEAD_SIZE, width + (kv_head + 1) * HEAD_SIZE)
        q = heads_of_query[:, kv_head]
        pre_scores = (
            jnp.einsum("qgd,kd->gqk", q, prefix[:, cols], preferred_element_type=jnp.float32)
            * score_scale
        )
        suf_scores = (
            jnp.einsum("qgd,kd->gqk", q, suffix[:, cols], preferred_element_type=jnp.float32)
            * score_scale
        )
        suf_scores = jnp.where(visible[None], suf_scores, MASKED_SCORE)
        peak = jnp.maximum(jnp.max(pre_scores, axis=-1), jnp.max(suf_scores, axis=-1))
        pre_weights = jnp.exp(pre_scores - peak[..., None])
        suf_weights = jnp.where(visible[None], jnp.exp(suf_scores - peak[..., None]), 0.0)
        total = jnp.sum(pre_weights, axis=-1) + jnp.sum(suf_weights, axis=-1)
        summed = jnp.einsum(
            "gqk,kd->gqd",
            pre_weights.astype(jnp.bfloat16),
            prefix[:, vcols],
            preferred_element_type=jnp.float32,
        ) + jnp.einsum(
            "gqk,kd->gqd",
            suf_weights.astype(jnp.bfloat16),
            suffix[:, vcols],
            preferred_element_type=jnp.float32,
        )
        return summed / total[..., None]

    attended = jnp.stack([one_head(h) for h in range(kv_heads)])
    attn = (
        jnp.transpose(attended, (2, 0, 1, 3))
        .reshape(tok_rows, q_heads * HEAD_SIZE)
        .astype(jnp.bfloat16)
    )
    swap = [(0, 1), (1, 0)]
    core = lax.axis_index("core")
    both = jnp.concatenate((attn, lax.ppermute(attn, "core", swap)), axis=0)
    weight = lax.all_gather(out_weight, BLK[:-1], axis=1, tiled=True)
    product = jnp.dot(both, weight, preferred_element_type=jnp.float32)
    reduced = lax.psum_scatter(product.astype(jnp.bfloat16), "mp", scatter_dimension=1, tiled=True)
    other = lax.ppermute(reduced[tok_rows:], "core", swap)
    mine = reduced[:tok_rows]
    per_block = out_weight.shape[1]
    mine = mine.reshape(tok_rows, -1, per_block)
    other = other.reshape(tok_rows, -1, per_block)
    even = jnp.where(core == 0, mine, other)
    odd = jnp.where(core == 0, other, mine)
    return jnp.stack((even, odd), axis=2).reshape(tok_rows, -1)


def solution(mesh):
    sizes = tuple(size for _, size in BLK_PARTS)
    split = jax.sharding.Mesh(
        mesh.devices.reshape(sizes + (mesh.shape["mp"],)), BLK + ("mp",)
    )
    placed = (
        P(BLK, "mp"),
        P(BLK, "mp"),
        P(BLK, "mp"),
        P(BLK, "mp"),
        P(BLK, "mp"),
        P("mp", BLK),
        P(),
    )
    return jax.shard_map(
        per_device, mesh=split, in_specs=placed, out_specs=P(BLK, "mp"), check_vma=False
    )
```

```python
import math

import jax
import jax.numpy as jnp
from jax import lax
from jax.sharding import PartitionSpec as P

HEAD_SIZE = 128


MASKED_SCORE = -1e30


BLK_PARTS = (("y", 4), ("x", 4), ("zh", 2), ("core", 2))
BLK = tuple(name for name, _ in BLK_PARTS)
BLOCKS = math.prod(size for _, size in BLK_PARTS)


def shifted(block, axis, distance):
    devices = BLOCKS
    route = [((i - distance) % devices, i) for i in range(devices)]
    return lax.ppermute(block, axis, route)


def shifted_pair(first, second, axis, distance):
    rows = first.shape[0] * first.shape[1]
    packed = jnp.concatenate(
        (first.reshape(rows, first.shape[2]), second.reshape(-1, second.shape[2])), axis=0
    )
    packed = shifted(packed, axis, distance)
    return (
        packed[:rows].reshape(first.shape),
        packed[rows:].reshape(second.shape),
    )


def per_device(
    queries,
    suffix_key_rows,
    suffix_value_rows,
    shared_prefix_keys,
    shared_prefix_values,
    out_weight,
    lengths,
):
    tok_rows = queries.shape[0]
    kv_heads = suffix_key_rows.shape[1] // HEAD_SIZE
    q_heads = queries.shape[1] // HEAD_SIZE
    heads_per_group = q_heads // kv_heads
    blocks = BLOCKS
    my_block = lax.axis_index(BLK)
    score_scale = 1.0 / math.sqrt(HEAD_SIZE)
    width = kv_heads * HEAD_SIZE

    own_kv = jnp.concatenate((suffix_key_rows, suffix_value_rows), axis=1)[None]
    prefix = jnp.concatenate((shared_prefix_keys, shared_prefix_values), axis=1)[None]
    suffix = own_kv
    reach = blocks // 4
    shifts = [1 << k for k in range(reach.bit_length() - 1)]
    shifts = shifts[1:2] + shifts[:1] + shifts[2:][::-1]
    distances = [0]
    for distance in shifts:
        got_suffix, got_prefix = shifted_pair(suffix, prefix, BLK, distance)
        suffix = jnp.concatenate((got_suffix, suffix), axis=0)
        prefix = jnp.concatenate((got_prefix, prefix), axis=0)
        distances = [d + distance for d in distances] + distances
    got_suffix, got_prefix = shifted_pair(own_kv, prefix, BLK, reach)
    suffix = jnp.concatenate((got_suffix, suffix), axis=0)
    prefix = jnp.concatenate((got_prefix, prefix), axis=0)
    distances = [reach] + distances
    distance = 2 * reach
    while distance < blocks:
        prefix = jnp.concatenate((shifted(prefix, BLK, distance), prefix), axis=0)
        distance *= 2

    count = suffix.shape[0]
    suffix = suffix.reshape(count * tok_rows, 2 * width)
    prefix = prefix.reshape(-1, 2 * width)

    req_ends = jnp.cumsum(lengths)
    local_rows = jnp.arange(tok_rows, dtype=jnp.int32)
    query_pos = my_block * tok_rows + local_rows

    def owner_of(position):
        return jnp.sum((position[:, None] >= req_ends[None, :]).astype(jnp.int32), axis=1)

    query_owner = owner_of(query_pos)
    block_of_key = my_block - jnp.repeat(jnp.array(distances, jnp.int32), tok_rows)
    key_pos = block_of_key * tok_rows + jnp.tile(local_rows, count)
    key_owner = owner_of(key_pos)
    visible = (
        (key_owner[None, :] == query_owner[:, None])
        & (key_pos[None, :] <= query_pos[:, None])
        & (key_pos[None, :] >= 0)
    )

    heads_of_query = queries.reshape(tok_rows, kv_heads, heads_per_group, HEAD_SIZE)

    def one_head(kv_head):
        cols = slice(kv_head * HEAD_SIZE, (kv_head + 1) * HEAD_SIZE)
        vcols = slice(width + kv_head * HEAD_SIZE, width + (kv_head + 1) * HEAD_SIZE)
        q = heads_of_query[:, kv_head]
        pre_scores = (
            jnp.einsum("qgd,kd->gqk", q, prefix[:, cols], preferred_element_type=jnp.float32)
            * score_scale
        )
        suf_scores = (
            jnp.einsum("qgd,kd->gqk", q, suffix[:, cols], preferred_element_type=jnp.float32)
            * score_scale
        )
        suf_scores = jnp.where(visible[None], suf_scores, MASKED_SCORE)
        peak = jnp.maximum(jnp.max(pre_scores, axis=-1), jnp.max(suf_scores, axis=-1))
        pre_weights = jnp.exp(pre_scores - peak[..., None])
        suf_weights = jnp.where(visible[None], jnp.exp(suf_scores - peak[..., None]), 0.0)
        total = jnp.sum(pre_weights, axis=-1) + jnp.sum(suf_weights, axis=-1)
        summed = jnp.einsum(
            "gqk,kd->gqd",
            pre_weights.astype(jnp.bfloat16),
            prefix[:, vcols],
            preferred_element_type=jnp.float32,
        ) + jnp.einsum(
            "gqk,kd->gqd",
            suf_weights.astype(jnp.bfloat16),
            suffix[:, vcols],
            preferred_element_type=jnp.float32,
        )
        return summed / total[..., None]

    attended = jnp.stack([one_head(h) for h in range(kv_heads)])
    attn = (
        jnp.transpose(attended, (2, 0, 1, 3))
        .reshape(tok_rows, q_heads * HEAD_SIZE)
        .astype(jnp.bfloat16)
    )
    swap = [(0, 1), (1, 0)]
    core = lax.axis_index("core")
    both = jnp.concatenate((attn, lax.ppermute(attn, "core", swap)), axis=0)
    weight = out_weight
    for name in BLK[-2::-1]:
        weight = lax.all_gather(weight, name, axis=1, tiled=True)
    product = jnp.dot(both, weight, preferred_element_type=jnp.float32)
    reduced = lax.psum_scatter(product.astype(jnp.bfloat16), "mp", scatter_dimension=1, tiled=True)
    other = lax.ppermute(reduced[tok_rows:], "core", swap)
    mine = reduced[:tok_rows]
    per_block = out_weight.shape[1]
    mine = mine.reshape(tok_rows, -1, per_block)
    other = other.reshape(tok_rows, -1, per_block)
    even = jnp.where(core == 0, mine, other)
    odd = jnp.where(core == 0, other, mine)
    return jnp.stack((even, odd), axis=2).reshape(tok_rows, -1)


def solution(mesh):
    sizes = tuple(size for _, size in BLK_PARTS)
    split = jax.sharding.Mesh(
        mesh.devices.reshape(sizes + (mesh.shape["mp"],)), BLK + ("mp",)
    )
    placed = (
        P(BLK, "mp"),
        P(BLK, "mp"),
        P(BLK, "mp"),
        P(BLK, "mp"),
        P(BLK, "mp"),
        P("mp", BLK),
        P(),
    )
    return jax.shard_map(
        per_device, mesh=split, in_specs=placed, out_specs=P(BLK, "mp"), check_vma=False
    )
```

```python
import math

import jax
import jax.numpy as jnp
from jax import lax
from jax.sharding import PartitionSpec as P

HEAD_SIZE = 128


MASKED_SCORE = -1e30


BLK_PARTS = (("y", 4), ("x", 4), ("zh", 2), ("core", 2))
BLK = tuple(name for name, _ in BLK_PARTS)
BLOCKS = math.prod(size for _, size in BLK_PARTS)


def shifted(block, axis, distance):
    devices = BLOCKS
    route = [((i - distance) % devices, i) for i in range(devices)]
    return lax.ppermute(block, axis, route)


def shifted_pair(first, second, axis, distance):
    rows = first.shape[0] * first.shape[1]
    packed = jnp.concatenate(
        (first.reshape(rows, first.shape[2]), second.reshape(-1, second.shape[2])), axis=0
    )
    packed = shifted(packed, axis, distance)
    return (
        packed[:rows].reshape(first.shape),
        packed[rows:].reshape(second.shape),
    )


def per_device(
    queries,
    suffix_key_rows,
    suffix_value_rows,
    shared_prefix_keys,
    shared_prefix_values,
    out_weight,
    lengths,
):
    tok_rows = queries.shape[0]
    kv_heads = suffix_key_rows.shape[1] // HEAD_SIZE
    q_heads = queries.shape[1] // HEAD_SIZE
    heads_per_group = q_heads // kv_heads
    blocks = BLOCKS
    my_block = lax.axis_index(BLK)
    score_scale = 1.0 / math.sqrt(HEAD_SIZE)
    width = kv_heads * HEAD_SIZE

    own_kv = jnp.concatenate((suffix_key_rows, suffix_value_rows), axis=1)[None]
    prefix = jnp.concatenate((shared_prefix_keys, shared_prefix_values), axis=1)[None]
    suffix = own_kv
    reach = blocks // 4
    shifts = [1 << k for k in range(reach.bit_length() - 1)]
    shifts = shifts[1:2] + shifts[:1] + shifts[2:][::-1]
    distances = [0]
    for distance in shifts:
        got_suffix, got_prefix = shifted_pair(suffix, prefix, BLK, distance)
        suffix = jnp.concatenate((got_suffix, suffix), axis=0)
        prefix = jnp.concatenate((got_prefix, prefix), axis=0)
        distances = [d + distance for d in distances] + distances
    got_suffix, got_prefix = shifted_pair(own_kv, prefix, BLK, reach)
    suffix = jnp.concatenate((got_suffix, suffix), axis=0)
    prefix = jnp.concatenate((got_prefix, prefix), axis=0)
    distances = [reach] + distances
    early_count = prefix.shape[0]
    distance = 2 * reach
    while distance < blocks:
        prefix = jnp.concatenate((shifted(prefix, BLK, distance), prefix), axis=0)
        distance *= 2

    count = suffix.shape[0]
    suffix = suffix.reshape(count * tok_rows, 2 * width)
    early_prefix = prefix[prefix.shape[0] - early_count:].reshape(-1, 2 * width)
    late_prefix = prefix[: prefix.shape[0] - early_count].reshape(-1, 2 * width)

    req_ends = jnp.cumsum(lengths)
    local_rows = jnp.arange(tok_rows, dtype=jnp.int32)
    query_pos = my_block * tok_rows + local_rows

    def owner_of(position):
        return jnp.sum((position[:, None] >= req_ends[None, :]).astype(jnp.int32), axis=1)

    query_owner = owner_of(query_pos)
    block_of_key = my_block - jnp.repeat(jnp.array(distances, jnp.int32), tok_rows)
    key_pos = block_of_key * tok_rows + jnp.tile(local_rows, count)
    key_owner = owner_of(key_pos)
    visible = (
        (key_owner[None, :] == query_owner[:, None])
        & (key_pos[None, :] <= query_pos[:, None])
        & (key_pos[None, :] >= 0)
    )

    heads_of_query = queries.reshape(tok_rows, kv_heads, heads_per_group, HEAD_SIZE)

    def scores_of(q, keys):
        return (
            jnp.einsum("qgd,kd->gqk", q, keys, preferred_element_type=jnp.float32) * score_scale
        )

    def weighted(weights, values):
        return jnp.einsum(
            "gqk,kd->gqd", weights.astype(jnp.bfloat16), values, preferred_element_type=jnp.float32
        )

    def one_head(kv_head):
        cols = slice(kv_head * HEAD_SIZE, (kv_head + 1) * HEAD_SIZE)
        vcols = slice(width + kv_head * HEAD_SIZE, width + (kv_head + 1) * HEAD_SIZE)
        q = heads_of_query[:, kv_head]
        pre_scores = scores_of(q, early_prefix[:, cols])
        suf_scores = jnp.where(visible[None], scores_of(q, suffix[:, cols]), MASKED_SCORE)
        first_peak = jnp.maximum(jnp.max(pre_scores, axis=-1), jnp.max(suf_scores, axis=-1))
        pre_weights = jnp.exp(pre_scores - first_peak[..., None])
        suf_weights = jnp.where(visible[None], jnp.exp(suf_scores - first_peak[..., None]), 0.0)
        first_total = jnp.sum(pre_weights, axis=-1) + jnp.sum(suf_weights, axis=-1)
        first_sum = weighted(pre_weights, early_prefix[:, vcols]) + weighted(
            suf_weights, suffix[:, vcols]
        )
        late_scores = scores_of(q, late_prefix[:, cols])
        late_peak = jnp.max(late_scores, axis=-1)
        late_weights = jnp.exp(late_scores - late_peak[..., None])
        late_total = jnp.sum(late_weights, axis=-1)
        late_sum = weighted(late_weights, late_prefix[:, vcols])
        peak = jnp.maximum(first_peak, late_peak)
        first_scale = jnp.exp(first_peak - peak)
        late_scale = jnp.exp(late_peak - peak)
        total = first_total * first_scale + late_total * late_scale
        summed = first_sum * first_scale[..., None] + late_sum * late_scale[..., None]
        return summed / total[..., None]

    attended = jnp.stack([one_head(h) for h in range(kv_heads)])
    attn = (
        jnp.transpose(attended, (2, 0, 1, 3))
        .reshape(tok_rows, q_heads * HEAD_SIZE)
        .astype(jnp.bfloat16)
    )
    swap = [(0, 1), (1, 0)]
    core = lax.axis_index("core")
    both = jnp.concatenate((attn, lax.ppermute(attn, "core", swap)), axis=0)
    weight = out_weight
    for name in BLK[-2::-1]:
        weight = lax.all_gather(weight, name, axis=1, tiled=True)
    product = jnp.dot(both, weight, preferred_element_type=jnp.float32)
    reduced = lax.psum_scatter(product.astype(jnp.bfloat16), "mp", scatter_dimension=1, tiled=True)
    other = lax.ppermute(reduced[tok_rows:], "core", swap)
    mine = reduced[:tok_rows]
    per_block = out_weight.shape[1]
    mine = mine.reshape(tok_rows, -1, per_block)
    other = other.reshape(tok_rows, -1, per_block)
    even = jnp.where(core == 0, mine, other)
    odd = jnp.where(core == 0, other, mine)
    return jnp.stack((even, odd), axis=2).reshape(tok_rows, -1)


def solution(mesh):
    sizes = tuple(size for _, size in BLK_PARTS)
    split = jax.sharding.Mesh(
        mesh.devices.reshape(sizes + (mesh.shape["mp"],)), BLK + ("mp",)
    )
    placed = (
        P(BLK, "mp"),
        P(BLK, "mp"),
        P(BLK, "mp"),
        P(BLK, "mp"),
        P(BLK, "mp"),
        P("mp", BLK),
        P(),
    )
    return jax.shard_map(
        per_device, mesh=split, in_specs=placed, out_specs=P(BLK, "mp"), check_vma=False
    )
```

```python
import math

import jax
import jax.numpy as jnp
from jax import lax
from jax.sharding import PartitionSpec as P

HEAD_SIZE = 128


MASKED_SCORE = -1e30


BLK_PARTS = (("y", 4), ("x", 4), ("zh", 2), ("core", 2))
BLK = tuple(name for name, _ in BLK_PARTS)
BLOCKS = math.prod(size for _, size in BLK_PARTS)


def shifted(block, axis, distance):
    devices = BLOCKS
    route = [((i - distance) % devices, i) for i in range(devices)]
    return lax.ppermute(block, axis, route)


def shifted_pair(first, second, axis, distance):
    rows = first.shape[0] * first.shape[1]
    packed = jnp.concatenate(
        (first.reshape(rows, first.shape[2]), second.reshape(-1, second.shape[2])), axis=0
    )
    packed = shifted(packed, axis, distance)
    return (
        packed[:rows].reshape(first.shape),
        packed[rows:].reshape(second.shape),
    )


def per_device(
    queries,
    suffix_key_rows,
    suffix_value_rows,
    shared_prefix_keys,
    shared_prefix_values,
    out_weight,
    lengths,
):
    tok_rows = queries.shape[0]
    kv_heads = suffix_key_rows.shape[1] // HEAD_SIZE
    q_heads = queries.shape[1] // HEAD_SIZE
    heads_per_group = q_heads // kv_heads
    blocks = BLOCKS
    my_block = lax.axis_index(BLK)
    score_scale = 1.0 / math.sqrt(HEAD_SIZE)
    width = kv_heads * HEAD_SIZE

    own_kv = jnp.concatenate((suffix_key_rows, suffix_value_rows), axis=1)[None]
    prefix = jnp.concatenate((shared_prefix_keys, shared_prefix_values), axis=1)[None]
    suffix = own_kv
    reach = blocks // 4
    distances = [0]
    step = 1
    while step < reach:
        got = [shifted_pair(suffix, prefix, BLK, step * k) for k in (1, 2, 3)]
        suffix = jnp.concatenate([pair[0] for pair in got] + [suffix], axis=0)
        prefix = jnp.concatenate([pair[1] for pair in got] + [prefix], axis=0)
        distances = [d + step * k for k in (1, 2, 3) for d in distances] + distances
        step *= 4
    late_suffix, got_prefix = shifted_pair(own_kv, prefix, BLK, reach)
    late_prefix = jnp.concatenate(
        [got_prefix]
        + [shifted(prefix, BLK, distance) for distance in range(2 * reach, blocks, reach)],
        axis=0,
    )
    count = suffix.shape[0]
    early_suffix = suffix.reshape(count * tok_rows, 2 * width)
    late_suffix = late_suffix.reshape(tok_rows, 2 * width)
    early_prefix = prefix.reshape(-1, 2 * width)
    late_prefix = late_prefix.reshape(-1, 2 * width)

    req_ends = jnp.cumsum(lengths)
    local_rows = jnp.arange(tok_rows, dtype=jnp.int32)
    query_pos = my_block * tok_rows + local_rows

    def owner_of(position):
        return jnp.sum((position[:, None] >= req_ends[None, :]).astype(jnp.int32), axis=1)

    query_owner = owner_of(query_pos)

    def visible_at(block_distances):
        block_of_key = my_block - jnp.repeat(jnp.array(block_distances, jnp.int32), tok_rows)
        key_pos = block_of_key * tok_rows + jnp.tile(local_rows, len(block_distances))
        key_owner = owner_of(key_pos)
        return (
            (key_owner[None, :] == query_owner[:, None])
            & (key_pos[None, :] <= query_pos[:, None])
            & (key_pos[None, :] >= 0)
        )

    early_visible = visible_at(distances)
    late_visible = visible_at([reach])

    heads_of_query = queries.reshape(tok_rows, kv_heads, heads_per_group, HEAD_SIZE)

    def scores_of(q, keys):
        return (
            jnp.einsum("qgd,kd->gqk", q, keys, preferred_element_type=jnp.float32) * score_scale
        )

    def weighted(weights, values):
        return jnp.einsum(
            "gqk,kd->gqd", weights.astype(jnp.bfloat16), values, preferred_element_type=jnp.float32
        )

    def piece(q, cols, vcols, prefix_rows, suffix_rows, visible):
        pre_scores = scores_of(q, prefix_rows[:, cols])
        suf_scores = jnp.where(visible[None], scores_of(q, suffix_rows[:, cols]), MASKED_SCORE)
        peak = jnp.maximum(jnp.max(pre_scores, axis=-1), jnp.max(suf_scores, axis=-1))
        pre_weights = jnp.exp(pre_scores - peak[..., None])
        suf_weights = jnp.where(visible[None], jnp.exp(suf_scores - peak[..., None]), 0.0)
        total = jnp.sum(pre_weights, axis=-1) + jnp.sum(suf_weights, axis=-1)
        summed = weighted(pre_weights, prefix_rows[:, vcols]) + weighted(
            suf_weights, suffix_rows[:, vcols]
        )
        return peak, total, summed

    def one_head(kv_head):
        cols = slice(kv_head * HEAD_SIZE, (kv_head + 1) * HEAD_SIZE)
        vcols = slice(width + kv_head * HEAD_SIZE, width + (kv_head + 1) * HEAD_SIZE)
        q = heads_of_query[:, kv_head]
        first_peak, first_total, first_sum = piece(
            q, cols, vcols, early_prefix, early_suffix, early_visible
        )
        late_peak, late_total, late_sum = piece(
            q, cols, vcols, late_prefix, late_suffix, late_visible
        )
        peak = jnp.maximum(first_peak, late_peak)
        first_scale = jnp.exp(first_peak - peak)
        late_scale = jnp.exp(late_peak - peak)
        total = first_total * first_scale + late_total * late_scale
        summed = first_sum * first_scale[..., None] + late_sum * late_scale[..., None]
        return summed / total[..., None]

    attended = jnp.stack([one_head(h) for h in range(kv_heads)])
    attn = (
        jnp.transpose(attended, (2, 0, 1, 3))
        .reshape(tok_rows, q_heads * HEAD_SIZE)
        .astype(jnp.bfloat16)
    )
    swap = [(0, 1), (1, 0)]
    core = lax.axis_index("core")
    both = jnp.concatenate((attn, lax.ppermute(attn, "core", swap)), axis=0)
    weight = out_weight
    for name in BLK[-2::-1]:
        weight = lax.all_gather(weight, name, axis=1, tiled=True)
    product = jnp.dot(both, weight, preferred_element_type=jnp.float32)
    reduced = lax.psum_scatter(product.astype(jnp.bfloat16), "mp", scatter_dimension=1, tiled=True)
    other = lax.ppermute(reduced[tok_rows:], "core", swap)
    mine = reduced[:tok_rows]
    per_block = out_weight.shape[1]
    mine = mine.reshape(tok_rows, -1, per_block)
    other = other.reshape(tok_rows, -1, per_block)
    even = jnp.where(core == 0, mine, other)
    odd = jnp.where(core == 0, other, mine)
    return jnp.stack((even, odd), axis=2).reshape(tok_rows, -1)


def solution(mesh):
    sizes = tuple(size for _, size in BLK_PARTS)
    split = jax.sharding.Mesh(
        mesh.devices.reshape(sizes + (mesh.shape["mp"],)), BLK + ("mp",)
    )
    placed = (
        P(BLK, "mp"),
        P(BLK, "mp"),
        P(BLK, "mp"),
        P(BLK, "mp"),
        P(BLK, "mp"),
        P("mp", BLK),
        P(),
    )
    return jax.shard_map(
        per_device, mesh=split, in_specs=placed, out_specs=P(BLK, "mp"), check_vma=False
    )
```

```python
import math

import jax
import jax.numpy as jnp
from jax import lax
from jax.sharding import PartitionSpec as P

HEAD_SIZE = 128


MASKED_SCORE = -1e30


BLK_PARTS = (("y", 4), ("x", 4), ("zh", 2), ("core", 2))
BLK = tuple(name for name, _ in BLK_PARTS)
BLOCKS = math.prod(size for _, size in BLK_PARTS)


def shifted(block, axis, distance):
    devices = BLOCKS
    route = [((i - distance) % devices, i) for i in range(devices)]
    return lax.ppermute(block, axis, route)


def shifted_pair(first, second, axis, distance):
    rows = first.shape[0] * first.shape[1]
    packed = jnp.concatenate(
        (first.reshape(rows, first.shape[2]), second.reshape(-1, second.shape[2])), axis=0
    )
    packed = shifted(packed, axis, distance)
    return (
        packed[:rows].reshape(first.shape),
        packed[rows:].reshape(second.shape),
    )


def per_device(
    queries,
    suffix_key_rows,
    suffix_value_rows,
    shared_prefix_keys,
    shared_prefix_values,
    out_weight,
    lengths,
):
    tok_rows = queries.shape[0]
    kv_heads = suffix_key_rows.shape[1] // HEAD_SIZE
    q_heads = queries.shape[1] // HEAD_SIZE
    heads_per_group = q_heads // kv_heads
    blocks = BLOCKS
    my_block = lax.axis_index(BLK)
    score_scale = 1.0 / math.sqrt(HEAD_SIZE)
    width = kv_heads * HEAD_SIZE

    own_kv = jnp.concatenate((suffix_key_rows, suffix_value_rows), axis=1)[None]
    prefix = jnp.concatenate((shared_prefix_keys, shared_prefix_values), axis=1)[None]
    suffix = own_kv
    reach = blocks // 4
    distances = [0]
    step = 1
    while step < reach:
        got = [shifted_pair(suffix, prefix, BLK, step * k) for k in (1, 2, 3)]
        suffix = jnp.concatenate([pair[0] for pair in got] + [suffix], axis=0)
        prefix = jnp.concatenate([pair[1] for pair in got] + [prefix], axis=0)
        distances = [d + step * k for k in (1, 2, 3) for d in distances] + distances
        step *= 4
    late_suffix, got_prefix = shifted_pair(own_kv, prefix, BLK, reach)
    late_prefix = jnp.concatenate(
        [got_prefix]
        + [shifted(prefix, BLK, distance) for distance in range(2 * reach, blocks, reach)],
        axis=0,
    )
    count = suffix.shape[0]
    early_suffix = suffix.reshape(count * tok_rows, 2 * width)
    late_suffix = late_suffix.reshape(tok_rows, 2 * width)
    early_prefix = prefix.reshape(-1, 2 * width)
    late_prefix = late_prefix.reshape(-1, 2 * width)

    req_ends = jnp.cumsum(lengths)
    local_rows = jnp.arange(tok_rows, dtype=jnp.int32)
    query_pos = my_block * tok_rows + local_rows

    def owner_of(position):
        return jnp.sum((position[:, None] >= req_ends[None, :]).astype(jnp.int32), axis=1)

    query_owner = owner_of(query_pos)

    def visible_at(block_distances):
        block_of_key = my_block - jnp.repeat(jnp.array(block_distances, jnp.int32), tok_rows)
        key_pos = block_of_key * tok_rows + jnp.tile(local_rows, len(block_distances))
        key_owner = owner_of(key_pos)
        return (
            (key_owner[None, :] == query_owner[:, None])
            & (key_pos[None, :] <= query_pos[:, None])
            & (key_pos[None, :] >= 0)
        )

    early_visible = visible_at(distances)
    late_visible = visible_at([reach])

    heads_of_query = queries.reshape(tok_rows, kv_heads, heads_per_group, HEAD_SIZE)

    def scores_of(q, keys):
        return (
            jnp.einsum("qgd,kd->gqk", q, keys, preferred_element_type=jnp.float32) * score_scale
        )

    def weighted(weights, values):
        return jnp.einsum(
            "gqk,kd->gqd", weights.astype(jnp.bfloat16), values, preferred_element_type=jnp.float32
        )

    def piece(q, cols, vcols, prefix_rows, suffix_rows, visible):
        pre_scores = scores_of(q, prefix_rows[:, cols])
        suf_scores = jnp.where(visible[None], scores_of(q, suffix_rows[:, cols]), MASKED_SCORE)
        peak = jnp.maximum(jnp.max(pre_scores, axis=-1), jnp.max(suf_scores, axis=-1))
        pre_weights = jnp.exp(pre_scores - peak[..., None])
        suf_weights = jnp.where(visible[None], jnp.exp(suf_scores - peak[..., None]), 0.0)
        total = jnp.sum(pre_weights, axis=-1) + jnp.sum(suf_weights, axis=-1)
        summed = weighted(pre_weights, prefix_rows[:, vcols]) + weighted(
            suf_weights, suffix_rows[:, vcols]
        )
        return peak, total, summed

    def one_head(kv_head):
        cols = slice(kv_head * HEAD_SIZE, (kv_head + 1) * HEAD_SIZE)
        vcols = slice(width + kv_head * HEAD_SIZE, width + (kv_head + 1) * HEAD_SIZE)
        q = heads_of_query[:, kv_head]
        first_peak, first_total, first_sum = piece(
            q, cols, vcols, early_prefix, early_suffix, early_visible
        )
        late_peak, late_total, late_sum = piece(
            q, cols, vcols, late_prefix, late_suffix, late_visible
        )
        peak = jnp.maximum(first_peak, late_peak)
        first_scale = jnp.exp(first_peak - peak)
        late_scale = jnp.exp(late_peak - peak)
        total = first_total * first_scale + late_total * late_scale
        summed = first_sum * first_scale[..., None] + late_sum * late_scale[..., None]
        return summed / total[..., None]

    attended = jnp.stack([one_head(h) for h in range(kv_heads)])
    attn = (
        jnp.transpose(attended, (2, 0, 1, 3))
        .reshape(tok_rows, q_heads * HEAD_SIZE)
        .astype(jnp.bfloat16)
    )
    swap = [(0, 1), (1, 0)]
    core = lax.axis_index("core")
    both = jnp.concatenate((attn, lax.ppermute(attn, "core", swap)), axis=0)
    z_hi = lax.axis_index(BLK[2])
    partner = lax.ppermute(out_weight, BLK[2], swap)
    pair = jnp.where(
        z_hi == 0,
        jnp.concatenate((out_weight, partner), axis=1),
        jnp.concatenate((partner, out_weight), axis=1),
    )
    across = dict(BLK_PARTS)[BLK[1]]
    from_behind = [pair] + [
        lax.ppermute(pair, BLK[1], [((i - k) % across, i) for i in range(across)])
        for k in range(1, across)
    ]
    in_order = jnp.roll(jnp.stack(from_behind[::-1]), lax.axis_index(BLK[1]) + 1, axis=0)
    row = jnp.moveaxis(in_order, 0, 1).reshape(out_weight.shape[0], -1)
    weight = lax.all_gather(row, BLK[0], axis=1, tiled=True)
    product = jnp.dot(both, weight, preferred_element_type=jnp.float32)
    reduced = lax.psum_scatter(product.astype(jnp.bfloat16), "mp", scatter_dimension=1, tiled=True)
    other = lax.ppermute(reduced[tok_rows:], "core", swap)
    mine = reduced[:tok_rows]
    per_block = out_weight.shape[1]
    mine = mine.reshape(tok_rows, -1, per_block)
    other = other.reshape(tok_rows, -1, per_block)
    even = jnp.where(core == 0, mine, other)
    odd = jnp.where(core == 0, other, mine)
    return jnp.stack((even, odd), axis=2).reshape(tok_rows, -1)


def solution(mesh):
    sizes = tuple(size for _, size in BLK_PARTS)
    split = jax.sharding.Mesh(
        mesh.devices.reshape(sizes + (mesh.shape["mp"],)), BLK + ("mp",)
    )
    placed = (
        P(BLK, "mp"),
        P(BLK, "mp"),
        P(BLK, "mp"),
        P(BLK, "mp"),
        P(BLK, "mp"),
        P("mp", BLK),
        P(),
    )
    return jax.shard_map(
        per_device, mesh=split, in_specs=placed, out_specs=P(BLK, "mp"), check_vma=False
    )
```

```python
import math

import jax
import jax.numpy as jnp
from jax import lax
from jax.sharding import PartitionSpec as P

HEAD_SIZE = 128


MASKED_SCORE = -1e30


BLK_PARTS = (("y", 4), ("x", 4), ("zh", 2), ("core", 2))
BLK = tuple(name for name, _ in BLK_PARTS)
BLOCKS = math.prod(size for _, size in BLK_PARTS)


def shifted(block, axis, distance):
    devices = BLOCKS
    route = [((i - distance) % devices, i) for i in range(devices)]
    return lax.ppermute(block, axis, route)


def shifted_pair(first, second, axis, distance):
    rows = first.shape[0] * first.shape[1]
    packed = jnp.concatenate(
        (first.reshape(rows, first.shape[2]), second.reshape(-1, second.shape[2])), axis=0
    )
    packed = shifted(packed, axis, distance)
    return (
        packed[:rows].reshape(first.shape),
        packed[rows:].reshape(second.shape),
    )


def per_device(
    queries,
    suffix_key_rows,
    suffix_value_rows,
    shared_prefix_keys,
    shared_prefix_values,
    out_weight,
    lengths,
):
    tok_rows = queries.shape[0]
    kv_heads = suffix_key_rows.shape[1] // HEAD_SIZE
    q_heads = queries.shape[1] // HEAD_SIZE
    heads_per_group = q_heads // kv_heads
    blocks = BLOCKS
    my_block = lax.axis_index(BLK)
    score_scale = 1.0 / math.sqrt(HEAD_SIZE)
    width = kv_heads * HEAD_SIZE

    own_kv = jnp.concatenate((suffix_key_rows, suffix_value_rows), axis=1)[None]
    prefix = jnp.concatenate((shared_prefix_keys, shared_prefix_values), axis=1)[None]
    suffix = own_kv
    reach = blocks // 4
    distances = [0]
    last_block = shifted(own_kv, BLK, reach)
    step = 1
    while step < reach:
        got = [shifted_pair(suffix, prefix, BLK, step * k) for k in (1, 2, 3)]
        suffix = jnp.concatenate([pair[0] for pair in got] + [suffix], axis=0)
        prefix = jnp.concatenate([pair[1] for pair in got] + [prefix], axis=0)
        distances = [d + step * k for k in (1, 2, 3) for d in distances] + distances
        step *= 4
    suffix = jnp.concatenate((last_block, suffix), axis=0)
    distances = [reach] + distances
    late_prefix = jnp.concatenate(
        [shifted(prefix, BLK, distance) for distance in range(reach, blocks, reach)], axis=0
    )
    count = suffix.shape[0]
    early_suffix = suffix.reshape(count * tok_rows, 2 * width)
    early_prefix = prefix.reshape(-1, 2 * width)
    late_prefix = late_prefix.reshape(-1, 2 * width)

    req_ends = jnp.cumsum(lengths)
    local_rows = jnp.arange(tok_rows, dtype=jnp.int32)
    query_pos = my_block * tok_rows + local_rows

    def owner_of(position):
        return jnp.sum((position[:, None] >= req_ends[None, :]).astype(jnp.int32), axis=1)

    query_owner = owner_of(query_pos)

    def visible_at(block_distances):
        block_of_key = my_block - jnp.repeat(jnp.array(block_distances, jnp.int32), tok_rows)
        key_pos = block_of_key * tok_rows + jnp.tile(local_rows, len(block_distances))
        key_owner = owner_of(key_pos)
        return (
            (key_owner[None, :] == query_owner[:, None])
            & (key_pos[None, :] <= query_pos[:, None])
            & (key_pos[None, :] >= 0)
        )

    early_visible = visible_at(distances)

    heads_of_query = queries.reshape(tok_rows, kv_heads, heads_per_group, HEAD_SIZE)

    def scores_of(q, keys):
        return (
            jnp.einsum("qgd,kd->gqk", q, keys, preferred_element_type=jnp.float32) * score_scale
        )

    def weighted(weights, values):
        return jnp.einsum(
            "gqk,kd->gqd", weights.astype(jnp.bfloat16), values, preferred_element_type=jnp.float32
        )

    def piece(q, cols, vcols, prefix_rows, suffix_rows, visible):
        pre_scores = scores_of(q, prefix_rows[:, cols])
        peak = jnp.max(pre_scores, axis=-1)
        if suffix_rows is not None:
            suf_scores = jnp.where(
                visible[None], scores_of(q, suffix_rows[:, cols]), MASKED_SCORE
            )
            peak = jnp.maximum(peak, jnp.max(suf_scores, axis=-1))
        pre_weights = jnp.exp(pre_scores - peak[..., None])
        total = jnp.sum(pre_weights, axis=-1)
        summed = weighted(pre_weights, prefix_rows[:, vcols])
        if suffix_rows is not None:
            suf_weights = jnp.where(visible[None], jnp.exp(suf_scores - peak[..., None]), 0.0)
            total = total + jnp.sum(suf_weights, axis=-1)
            summed = summed + weighted(suf_weights, suffix_rows[:, vcols])
        return peak, total, summed

    def one_head(kv_head):
        cols = slice(kv_head * HEAD_SIZE, (kv_head + 1) * HEAD_SIZE)
        vcols = slice(width + kv_head * HEAD_SIZE, width + (kv_head + 1) * HEAD_SIZE)
        q = heads_of_query[:, kv_head]
        first_peak, first_total, first_sum = piece(
            q, cols, vcols, early_prefix, early_suffix, early_visible
        )
        late_peak, late_total, late_sum = piece(q, cols, vcols, late_prefix, None, None)
        peak = jnp.maximum(first_peak, late_peak)
        first_scale = jnp.exp(first_peak - peak)
        late_scale = jnp.exp(late_peak - peak)
        total = first_total * first_scale + late_total * late_scale
        summed = first_sum * first_scale[..., None] + late_sum * late_scale[..., None]
        return summed / total[..., None]

    attended = jnp.stack([one_head(h) for h in range(kv_heads)])
    attn = (
        jnp.transpose(attended, (2, 0, 1, 3))
        .reshape(tok_rows, q_heads * HEAD_SIZE)
        .astype(jnp.bfloat16)
    )
    swap = [(0, 1), (1, 0)]
    core = lax.axis_index("core")
    both = jnp.concatenate((attn, lax.ppermute(attn, "core", swap)), axis=0)
    z_hi = lax.axis_index(BLK[2])
    partner = lax.ppermute(out_weight, BLK[2], swap)
    pair = jnp.where(
        z_hi == 0,
        jnp.concatenate((out_weight, partner), axis=1),
        jnp.concatenate((partner, out_weight), axis=1),
    )
    across = dict(BLK_PARTS)[BLK[1]]
    from_behind = [pair] + [
        lax.ppermute(pair, BLK[1], [((i - k) % across, i) for i in range(across)])
        for k in range(1, across)
    ]
    in_order = jnp.roll(jnp.stack(from_behind[::-1]), lax.axis_index(BLK[1]) + 1, axis=0)
    row = jnp.moveaxis(in_order, 0, 1).reshape(out_weight.shape[0], -1)
    weight = lax.all_gather(row, BLK[0], axis=1, tiled=True)
    product = jnp.dot(both, weight, preferred_element_type=jnp.float32)
    reduced = lax.psum_scatter(product.astype(jnp.bfloat16), "mp", scatter_dimension=1, tiled=True)
    other = lax.ppermute(reduced[tok_rows:], "core", swap)
    mine = reduced[:tok_rows]
    per_block = out_weight.shape[1]
    mine = mine.reshape(tok_rows, -1, per_block)
    other = other.reshape(tok_rows, -1, per_block)
    even = jnp.where(core == 0, mine, other)
    odd = jnp.where(core == 0, other, mine)
    return jnp.stack((even, odd), axis=2).reshape(tok_rows, -1)


def solution(mesh):
    sizes = tuple(size for _, size in BLK_PARTS)
    split = jax.sharding.Mesh(
        mesh.devices.reshape(sizes + (mesh.shape["mp"],)), BLK + ("mp",)
    )
    placed = (
        P(BLK, "mp"),
        P(BLK, "mp"),
        P(BLK, "mp"),
        P(BLK, "mp"),
        P(BLK, "mp"),
        P("mp", BLK),
        P(),
    )
    return jax.shard_map(
        per_device, mesh=split, in_specs=placed, out_specs=P(BLK, "mp"), check_vma=False
    )
```

```python
import math

import jax
import jax.numpy as jnp
from jax import lax
from jax.sharding import PartitionSpec as P

HEAD_SIZE = 128


MASKED_SCORE = -1e30


BLK_PARTS = (("y", 4), ("x", 4), ("zh", 2), ("core", 2))
BLK = tuple(name for name, _ in BLK_PARTS)
BLOCKS = math.prod(size for _, size in BLK_PARTS)


def shifted(block, axis, distance):
    devices = BLOCKS
    route = [((i - distance) % devices, i) for i in range(devices)]
    return lax.ppermute(block, axis, route)


def shifted_pair(first, second, axis, distance):
    rows = first.shape[0] * first.shape[1]
    packed = jnp.concatenate(
        (first.reshape(rows, first.shape[2]), second.reshape(-1, second.shape[2])), axis=0
    )
    packed = shifted(packed, axis, distance)
    return (
        packed[:rows].reshape(first.shape),
        packed[rows:].reshape(second.shape),
    )


def per_device(
    queries,
    suffix_key_rows,
    suffix_value_rows,
    shared_prefix_keys,
    shared_prefix_values,
    out_weight,
    lengths,
):
    tok_rows = queries.shape[0]
    kv_heads = suffix_key_rows.shape[1] // HEAD_SIZE
    q_heads = queries.shape[1] // HEAD_SIZE
    heads_per_group = q_heads // kv_heads
    blocks = BLOCKS
    my_block = lax.axis_index(BLK)
    score_scale = 1.0 / math.sqrt(HEAD_SIZE)
    width = kv_heads * HEAD_SIZE

    own_kv = jnp.concatenate((suffix_key_rows, suffix_value_rows), axis=1)[None]
    prefix = jnp.concatenate((shared_prefix_keys, shared_prefix_values), axis=1)[None]
    suffix = own_kv
    reach = blocks // 4
    distances = [0]
    step = 1
    while step < reach:
        got = [shifted_pair(suffix, prefix, BLK, step * k) for k in (1, 2, 3)]
        suffix = jnp.concatenate([pair[0] for pair in got] + [suffix], axis=0)
        prefix = jnp.concatenate([pair[1] for pair in got] + [prefix], axis=0)
        distances = [d + step * k for k in (1, 2, 3) for d in distances] + distances
        step *= 4
    late_suffix, got_prefix = shifted_pair(own_kv, prefix, BLK, reach)
    late_prefix = jnp.concatenate(
        [got_prefix]
        + [shifted(prefix, BLK, distance) for distance in range(2 * reach, blocks, reach)],
        axis=0,
    )
    count = suffix.shape[0]
    early_suffix = suffix.reshape(count * tok_rows, 2 * width)
    late_suffix = late_suffix.reshape(tok_rows, 2 * width)
    early_prefix = prefix.reshape(-1, 2 * width)
    late_prefix = late_prefix.reshape(-1, 2 * width)

    req_ends = jnp.cumsum(lengths)
    local_rows = jnp.arange(tok_rows, dtype=jnp.int32)
    query_pos = my_block * tok_rows + local_rows

    def owner_of(position):
        return jnp.sum((position[:, None] >= req_ends[None, :]).astype(jnp.int32), axis=1)

    query_owner = owner_of(query_pos)

    def visible_at(block_distances):
        block_of_key = my_block - jnp.repeat(jnp.array(block_distances, jnp.int32), tok_rows)
        key_pos = block_of_key * tok_rows + jnp.tile(local_rows, len(block_distances))
        key_owner = owner_of(key_pos)
        return (
            (key_owner[None, :] == query_owner[:, None])
            & (key_pos[None, :] <= query_pos[:, None])
            & (key_pos[None, :] >= 0)
        )

    early_visible = visible_at(distances)
    late_visible = visible_at([reach])

    heads_of_query = queries.reshape(tok_rows, kv_heads, heads_per_group, HEAD_SIZE)

    def scores_of(q, keys):
        return (
            jnp.einsum("qgd,kd->gqk", q, keys, preferred_element_type=jnp.float32) * score_scale
        )

    def weighted(weights, values):
        return jnp.einsum(
            "gqk,kd->gqd", weights.astype(jnp.bfloat16), values, preferred_element_type=jnp.float32
        )

    def piece(q, cols, vcols, prefix_rows, suffix_rows, visible):
        pre_scores = scores_of(q, prefix_rows[:, cols])
        suf_scores = jnp.where(visible[None], scores_of(q, suffix_rows[:, cols]), MASKED_SCORE)
        peak = jnp.maximum(jnp.max(pre_scores, axis=-1), jnp.max(suf_scores, axis=-1))
        pre_weights = jnp.exp(pre_scores - peak[..., None])
        suf_weights = jnp.where(visible[None], jnp.exp(suf_scores - peak[..., None]), 0.0)
        total = jnp.sum(pre_weights, axis=-1) + jnp.sum(suf_weights, axis=-1)
        summed = weighted(pre_weights, prefix_rows[:, vcols]) + weighted(
            suf_weights, suffix_rows[:, vcols]
        )
        return peak, total, summed

    def one_head(kv_head):
        cols = slice(kv_head * HEAD_SIZE, (kv_head + 1) * HEAD_SIZE)
        vcols = slice(width + kv_head * HEAD_SIZE, width + (kv_head + 1) * HEAD_SIZE)
        q = heads_of_query[:, kv_head]
        first_peak, first_total, first_sum = piece(
            q, cols, vcols, early_prefix, early_suffix, early_visible
        )
        late_peak, late_total, late_sum = piece(
            q, cols, vcols, late_prefix, late_suffix, late_visible
        )
        peak = jnp.maximum(first_peak, late_peak)
        first_scale = jnp.exp(first_peak - peak)
        late_scale = jnp.exp(late_peak - peak)
        total = first_total * first_scale + late_total * late_scale
        summed = first_sum * first_scale[..., None] + late_sum * late_scale[..., None]
        return summed / total[..., None]

    attended = jnp.stack([one_head(h) for h in range(kv_heads)])
    attn = (
        jnp.transpose(attended, (2, 0, 1, 3))
        .reshape(tok_rows, q_heads * HEAD_SIZE)
        .astype(jnp.bfloat16)
    )
    swap = [(0, 1), (1, 0)]
    core = lax.axis_index("core")
    both = jnp.concatenate((attn, lax.ppermute(attn, "core", swap)), axis=0)
    across = dict(BLK_PARTS)[BLK[1]]
    from_behind = [out_weight] + [
        lax.ppermute(out_weight, BLK[1], [((i - k) % across, i) for i in range(across)])
        for k in range(1, across)
    ]
    in_order = jnp.roll(jnp.stack(from_behind[::-1]), lax.axis_index(BLK[1]) + 1, axis=0)
    row = jnp.moveaxis(in_order, 0, 1).reshape(out_weight.shape[0], -1)
    weight = lax.all_gather(row, (BLK[0], BLK[2]), axis=1, tiled=True)
    weight = weight.reshape(
        out_weight.shape[0], dict(BLK_PARTS)[BLK[0]], dict(BLK_PARTS)[BLK[2]], across, -1
    )
    weight = jnp.swapaxes(weight, 2, 3).reshape(out_weight.shape[0], -1)
    product = jnp.dot(both, weight, preferred_element_type=jnp.float32)
    reduced = lax.psum_scatter(product.astype(jnp.bfloat16), "mp", scatter_dimension=1, tiled=True)
    other = lax.ppermute(reduced[tok_rows:], "core", swap)
    mine = reduced[:tok_rows]
    per_block = out_weight.shape[1]
    mine = mine.reshape(tok_rows, -1, per_block)
    other = other.reshape(tok_rows, -1, per_block)
    even = jnp.where(core == 0, mine, other)
    odd = jnp.where(core == 0, other, mine)
    return jnp.stack((even, odd), axis=2).reshape(tok_rows, -1)


def solution(mesh):
    sizes = tuple(size for _, size in BLK_PARTS)
    split = jax.sharding.Mesh(
        mesh.devices.reshape(sizes + (mesh.shape["mp"],)), BLK + ("mp",)
    )
    placed = (
        P(BLK, "mp"),
        P(BLK, "mp"),
        P(BLK, "mp"),
        P(BLK, "mp"),
        P(BLK, "mp"),
        P("mp", BLK),
        P(),
    )
    return jax.shard_map(
        per_device, mesh=split, in_specs=placed, out_specs=P(BLK, "mp"), check_vma=False
    )
```

```python
import math

import jax
import jax.numpy as jnp
from jax import lax
from jax.sharding import PartitionSpec as P

HEAD_SIZE = 128


MASKED_SCORE = -1e30


BLK_PARTS = (("y", 4), ("x", 4), ("zh", 2), ("core", 2))
BLK = tuple(name for name, _ in BLK_PARTS)
BLOCKS = math.prod(size for _, size in BLK_PARTS)


def shifted(block, axis, distance):
    devices = BLOCKS
    route = [((i - distance) % devices, i) for i in range(devices)]
    return lax.ppermute(block, axis, route)


def shifted_pair(first, second, axis, distance):
    rows = first.shape[0] * first.shape[1]
    packed = jnp.concatenate(
        (first.reshape(rows, first.shape[2]), second.reshape(-1, second.shape[2])), axis=0
    )
    packed = shifted(packed, axis, distance)
    return (
        packed[:rows].reshape(first.shape),
        packed[rows:].reshape(second.shape),
    )


def per_device(
    queries,
    suffix_key_rows,
    suffix_value_rows,
    shared_prefix_keys,
    shared_prefix_values,
    out_weight,
    lengths,
):
    tok_rows = queries.shape[0]
    kv_heads = suffix_key_rows.shape[1] // HEAD_SIZE
    q_heads = queries.shape[1] // HEAD_SIZE
    heads_per_group = q_heads // kv_heads
    blocks = BLOCKS
    my_block = lax.axis_index(BLK)
    score_scale = 1.0 / math.sqrt(HEAD_SIZE)
    width = kv_heads * HEAD_SIZE

    own_kv = jnp.concatenate((suffix_key_rows, suffix_value_rows), axis=1)[None]
    prefix = jnp.concatenate((shared_prefix_keys, shared_prefix_values), axis=1)[None]
    suffix = own_kv
    reach = blocks // 4
    distances = [0]
    step = 1
    while step < reach:
        got = [shifted_pair(suffix, prefix, BLK, step * k) for k in (1, 2, 3)]
        suffix = jnp.concatenate([pair[0] for pair in got] + [suffix], axis=0)
        prefix = jnp.concatenate([pair[1] for pair in got] + [prefix], axis=0)
        distances = [d + step * k for k in (1, 2, 3) for d in distances] + distances
        step *= 4
    late_suffix, got_prefix = shifted_pair(own_kv, prefix, BLK, reach)
    late_prefix = jnp.concatenate(
        [got_prefix]
        + [shifted(prefix, BLK, distance) for distance in range(2 * reach, blocks, reach)],
        axis=0,
    )
    count = suffix.shape[0]
    early_suffix = suffix.reshape(count * tok_rows, 2 * width)
    late_suffix = late_suffix.reshape(tok_rows, 2 * width)
    early_prefix = prefix.reshape(-1, 2 * width)
    late_prefix = late_prefix.reshape(-1, 2 * width)

    req_ends = jnp.cumsum(lengths)
    local_rows = jnp.arange(tok_rows, dtype=jnp.int32)
    query_pos = my_block * tok_rows + local_rows

    def owner_of(position):
        return jnp.sum((position[:, None] >= req_ends[None, :]).astype(jnp.int32), axis=1)

    query_owner = owner_of(query_pos)

    def visible_at(block_distances):
        block_of_key = my_block - jnp.repeat(jnp.array(block_distances, jnp.int32), tok_rows)
        key_pos = block_of_key * tok_rows + jnp.tile(local_rows, len(block_distances))
        key_owner = owner_of(key_pos)
        return (
            (key_owner[None, :] == query_owner[:, None])
            & (key_pos[None, :] <= query_pos[:, None])
            & (key_pos[None, :] >= 0)
        )

    early_visible = visible_at(distances)
    late_visible = visible_at([reach])

    heads_of_query = queries.reshape(tok_rows, kv_heads, heads_per_group, HEAD_SIZE)

    def scores_of(q, keys):
        return (
            jnp.einsum("qgd,kd->gqk", q, keys, preferred_element_type=jnp.float32) * score_scale
        )

    def weighted(weights, values):
        return jnp.einsum(
            "gqk,kd->gqd", weights.astype(jnp.bfloat16), values, preferred_element_type=jnp.float32
        )

    def piece(q, cols, vcols, prefix_rows, suffix_rows, visible):
        pre_scores = scores_of(q, prefix_rows[:, cols])
        suf_scores = jnp.where(visible[None], scores_of(q, suffix_rows[:, cols]), MASKED_SCORE)
        peak = jnp.maximum(jnp.max(pre_scores, axis=-1), jnp.max(suf_scores, axis=-1))
        pre_weights = jnp.exp(pre_scores - peak[..., None])
        suf_weights = jnp.where(visible[None], jnp.exp(suf_scores - peak[..., None]), 0.0)
        total = jnp.sum(pre_weights, axis=-1) + jnp.sum(suf_weights, axis=-1)
        summed = weighted(pre_weights, prefix_rows[:, vcols]) + weighted(
            suf_weights, suffix_rows[:, vcols]
        )
        return peak, total, summed

    def one_head(kv_head):
        cols = slice(kv_head * HEAD_SIZE, (kv_head + 1) * HEAD_SIZE)
        vcols = slice(width + kv_head * HEAD_SIZE, width + (kv_head + 1) * HEAD_SIZE)
        q = heads_of_query[:, kv_head]
        first_peak, first_total, first_sum = piece(
            q, cols, vcols, early_prefix, early_suffix, early_visible
        )
        late_peak, late_total, late_sum = piece(
            q, cols, vcols, late_prefix, late_suffix, late_visible
        )
        peak = jnp.maximum(first_peak, late_peak)
        first_scale = jnp.exp(first_peak - peak)
        late_scale = jnp.exp(late_peak - peak)
        total = first_total * first_scale + late_total * late_scale
        summed = first_sum * first_scale[..., None] + late_sum * late_scale[..., None]
        return summed / total[..., None]

    attended = jnp.stack([one_head(h) for h in range(kv_heads)])
    attn = (
        jnp.transpose(attended, (2, 0, 1, 3))
        .reshape(tok_rows, q_heads * HEAD_SIZE)
        .astype(jnp.bfloat16)
    )
    swap = [(0, 1), (1, 0)]
    core = lax.axis_index("core")
    both = jnp.concatenate((attn, lax.ppermute(attn, "core", swap)), axis=0)
    across = dict(BLK_PARTS)[BLK[1]]
    from_behind = [out_weight] + [
        lax.ppermute(out_weight, BLK[1], [((i - k) % across, i) for i in range(across)])
        for k in range(1, across)
    ]
    in_order = jnp.roll(jnp.stack(from_behind[::-1]), lax.axis_index(BLK[1]) + 1, axis=0)
    row = jnp.moveaxis(in_order, 0, 1)
    partner = lax.ppermute(row, BLK[2], swap)
    pair = jnp.where(
        lax.axis_index(BLK[2]) == 0,
        jnp.stack((row, partner), axis=2),
        jnp.stack((partner, row), axis=2),
    )
    weight = lax.all_gather(pair.reshape(out_weight.shape[0], -1), BLK[0], axis=1, tiled=True)
    product = jnp.dot(both, weight, preferred_element_type=jnp.float32)
    reduced = lax.psum_scatter(product.astype(jnp.bfloat16), "mp", scatter_dimension=1, tiled=True)
    other = lax.ppermute(reduced[tok_rows:], "core", swap)
    mine = reduced[:tok_rows]
    per_block = out_weight.shape[1]
    mine = mine.reshape(tok_rows, -1, per_block)
    other = other.reshape(tok_rows, -1, per_block)
    even = jnp.where(core == 0, mine, other)
    odd = jnp.where(core == 0, other, mine)
    return jnp.stack((even, odd), axis=2).reshape(tok_rows, -1)


def solution(mesh):
    sizes = tuple(size for _, size in BLK_PARTS)
    split = jax.sharding.Mesh(
        mesh.devices.reshape(sizes + (mesh.shape["mp"],)), BLK + ("mp",)
    )
    placed = (
        P(BLK, "mp"),
        P(BLK, "mp"),
        P(BLK, "mp"),
        P(BLK, "mp"),
        P(BLK, "mp"),
        P("mp", BLK),
        P(),
    )
    return jax.shard_map(
        per_device, mesh=split, in_specs=placed, out_specs=P(BLK, "mp"), check_vma=False
    )
```

```python
import math

import jax
import jax.numpy as jnp
from jax import lax
from jax.sharding import PartitionSpec as P

HEAD_SIZE = 128


MASKED_SCORE = -1e30


BLK_PARTS = (("y", 4), ("x", 4), ("zh", 2), ("core", 2))
BLK = tuple(name for name, _ in BLK_PARTS)
BLOCKS = math.prod(size for _, size in BLK_PARTS)


def shifted(block, axis, distance):
    devices = BLOCKS
    route = [((i - distance) % devices, i) for i in range(devices)]
    return lax.ppermute(block, axis, route)


def shifted_pair(first, second, axis, distance):
    rows = first.shape[0] * first.shape[1]
    packed = jnp.concatenate(
        (first.reshape(rows, first.shape[2]), second.reshape(-1, second.shape[2])), axis=0
    )
    packed = shifted(packed, axis, distance)
    return (
        packed[:rows].reshape(first.shape),
        packed[rows:].reshape(second.shape),
    )


def per_device(
    queries,
    suffix_key_rows,
    suffix_value_rows,
    shared_prefix_keys,
    shared_prefix_values,
    out_weight,
    lengths,
):
    tok_rows = queries.shape[0]
    kv_heads = suffix_key_rows.shape[1] // HEAD_SIZE
    q_heads = queries.shape[1] // HEAD_SIZE
    heads_per_group = q_heads // kv_heads
    blocks = BLOCKS
    my_block = lax.axis_index(BLK)
    score_scale = 1.0 / math.sqrt(HEAD_SIZE)
    width = kv_heads * HEAD_SIZE

    own_kv = jnp.concatenate((suffix_key_rows, suffix_value_rows), axis=1)[None]
    prefix = jnp.concatenate((shared_prefix_keys, shared_prefix_values), axis=1)[None]
    suffix = own_kv
    reach = blocks // 4
    distances = [0]
    step = 1
    while step < reach:
        if step > 1:
            own_kv, suffix, prefix = lax.optimization_barrier((own_kv, suffix, prefix))
            last_block = shifted(own_kv, BLK, reach)
        got = [shifted_pair(suffix, prefix, BLK, step * k) for k in (1, 2, 3)]
        suffix = jnp.concatenate([pair[0] for pair in got] + [suffix], axis=0)
        prefix = jnp.concatenate([pair[1] for pair in got] + [prefix], axis=0)
        distances = [d + step * k for k in (1, 2, 3) for d in distances] + distances
        step *= 4
    suffix = jnp.concatenate((last_block, suffix), axis=0)
    distances = [reach] + distances
    late_prefix = jnp.concatenate(
        [shifted(prefix, BLK, distance) for distance in range(reach, blocks, reach)], axis=0
    )
    count = suffix.shape[0]
    early_suffix = suffix.reshape(count * tok_rows, 2 * width)
    early_prefix = prefix.reshape(-1, 2 * width)
    late_prefix = late_prefix.reshape(-1, 2 * width)

    req_ends = jnp.cumsum(lengths)
    local_rows = jnp.arange(tok_rows, dtype=jnp.int32)
    query_pos = my_block * tok_rows + local_rows

    def owner_of(position):
        return jnp.sum((position[:, None] >= req_ends[None, :]).astype(jnp.int32), axis=1)

    query_owner = owner_of(query_pos)

    def visible_at(block_distances):
        block_of_key = my_block - jnp.repeat(jnp.array(block_distances, jnp.int32), tok_rows)
        key_pos = block_of_key * tok_rows + jnp.tile(local_rows, len(block_distances))
        key_owner = owner_of(key_pos)
        return (
            (key_owner[None, :] == query_owner[:, None])
            & (key_pos[None, :] <= query_pos[:, None])
            & (key_pos[None, :] >= 0)
        )

    early_visible = visible_at(distances)

    heads_of_query = queries.reshape(tok_rows, kv_heads, heads_per_group, HEAD_SIZE)

    def scores_of(q, keys):
        return (
            jnp.einsum("qgd,kd->gqk", q, keys, preferred_element_type=jnp.float32) * score_scale
        )

    def weighted(weights, values):
        return jnp.einsum(
            "gqk,kd->gqd", weights.astype(jnp.bfloat16), values, preferred_element_type=jnp.float32
        )

    def piece(q, cols, vcols, prefix_rows, suffix_rows, visible):
        pre_scores = scores_of(q, prefix_rows[:, cols])
        peak = jnp.max(pre_scores, axis=-1)
        if suffix_rows is not None:
            suf_scores = jnp.where(
                visible[None], scores_of(q, suffix_rows[:, cols]), MASKED_SCORE
            )
            peak = jnp.maximum(peak, jnp.max(suf_scores, axis=-1))
        pre_weights = jnp.exp(pre_scores - peak[..., None])
        total = jnp.sum(pre_weights, axis=-1)
        summed = weighted(pre_weights, prefix_rows[:, vcols])
        if suffix_rows is not None:
            suf_weights = jnp.where(visible[None], jnp.exp(suf_scores - peak[..., None]), 0.0)
            total = total + jnp.sum(suf_weights, axis=-1)
            summed = summed + weighted(suf_weights, suffix_rows[:, vcols])
        return peak, total, summed

    def one_head(kv_head):
        cols = slice(kv_head * HEAD_SIZE, (kv_head + 1) * HEAD_SIZE)
        vcols = slice(width + kv_head * HEAD_SIZE, width + (kv_head + 1) * HEAD_SIZE)
        q = heads_of_query[:, kv_head]
        first_peak, first_total, first_sum = piece(
            q, cols, vcols, early_prefix, early_suffix, early_visible
        )
        late_peak, late_total, late_sum = piece(q, cols, vcols, late_prefix, None, None)
        peak = jnp.maximum(first_peak, late_peak)
        first_scale = jnp.exp(first_peak - peak)
        late_scale = jnp.exp(late_peak - peak)
        total = first_total * first_scale + late_total * late_scale
        summed = first_sum * first_scale[..., None] + late_sum * late_scale[..., None]
        return summed / total[..., None]

    attended = jnp.stack([one_head(h) for h in range(kv_heads)])
    attn = (
        jnp.transpose(attended, (2, 0, 1, 3))
        .reshape(tok_rows, q_heads * HEAD_SIZE)
        .astype(jnp.bfloat16)
    )
    swap = [(0, 1), (1, 0)]
    core = lax.axis_index("core")
    both = jnp.concatenate((attn, lax.ppermute(attn, "core", swap)), axis=0)
    across = dict(BLK_PARTS)[BLK[1]]
    from_behind = [out_weight] + [
        lax.ppermute(out_weight, BLK[1], [((i - k) % across, i) for i in range(across)])
        for k in range(1, across)
    ]
    in_order = jnp.roll(jnp.stack(from_behind[::-1]), lax.axis_index(BLK[1]) + 1, axis=0)
    row = jnp.moveaxis(in_order, 0, 1)
    partner = lax.ppermute(row, BLK[2], swap)
    pair = jnp.where(
        lax.axis_index(BLK[2]) == 0,
        jnp.stack((row, partner), axis=2),
        jnp.stack((partner, row), axis=2),
    )
    weight = lax.all_gather(pair.reshape(out_weight.shape[0], -1), BLK[0], axis=1, tiled=True)
    product = jnp.dot(both, weight, preferred_element_type=jnp.float32)
    reduced = lax.psum_scatter(product.astype(jnp.bfloat16), "mp", scatter_dimension=1, tiled=True)
    other = lax.ppermute(reduced[tok_rows:], "core", swap)
    mine = reduced[:tok_rows]
    per_block = out_weight.shape[1]
    mine = mine.reshape(tok_rows, -1, per_block)
    other = other.reshape(tok_rows, -1, per_block)
    even = jnp.where(core == 0, mine, other)
    odd = jnp.where(core == 0, other, mine)
    return jnp.stack((even, odd), axis=2).reshape(tok_rows, -1)


def solution(mesh):
    sizes = tuple(size for _, size in BLK_PARTS)
    split = jax.sharding.Mesh(
        mesh.devices.reshape(sizes + (mesh.shape["mp"],)), BLK + ("mp",)
    )
    placed = (
        P(BLK, "mp"),
        P(BLK, "mp"),
        P(BLK, "mp"),
        P(BLK, "mp"),
        P(BLK, "mp"),
        P("mp", BLK),
        P(),
    )
    return jax.shard_map(
        per_device, mesh=split, in_specs=placed, out_specs=P(BLK, "mp"), check_vma=False
    )
```

```python
import math

import jax
import jax.numpy as jnp
from jax import lax
from jax.sharding import PartitionSpec as P

HEAD_SIZE = 128


MASKED_SCORE = -1e30


BLK_PARTS = (("y", 4), ("x", 4), ("zh", 2), ("core", 2))
BLK = tuple(name for name, _ in BLK_PARTS)
BLOCKS = math.prod(size for _, size in BLK_PARTS)


def shifted(block, axis, distance):
    devices = BLOCKS
    route = [((i - distance) % devices, i) for i in range(devices)]
    return lax.ppermute(block, axis, route)


def shifted_pair(first, second, axis, distance):
    rows = first.shape[0] * first.shape[1]
    packed = jnp.concatenate(
        (first.reshape(rows, first.shape[2]), second.reshape(-1, second.shape[2])), axis=0
    )
    packed = shifted(packed, axis, distance)
    return (
        packed[:rows].reshape(first.shape),
        packed[rows:].reshape(second.shape),
    )


def per_device(
    queries,
    suffix_key_rows,
    suffix_value_rows,
    shared_prefix_keys,
    shared_prefix_values,
    out_weight,
    lengths,
):
    tok_rows = queries.shape[0]
    kv_heads = suffix_key_rows.shape[1] // HEAD_SIZE
    q_heads = queries.shape[1] // HEAD_SIZE
    heads_per_group = q_heads // kv_heads
    blocks = BLOCKS
    my_block = lax.axis_index(BLK)
    score_scale = 1.0 / math.sqrt(HEAD_SIZE)
    width = kv_heads * HEAD_SIZE

    own_kv = jnp.concatenate((suffix_key_rows, suffix_value_rows), axis=1)[None]
    prefix = jnp.concatenate((shared_prefix_keys, shared_prefix_values), axis=1)[None]
    suffix = own_kv
    reach = blocks // 4
    distances = [0]
    step = 1
    while step < reach:
        got = [shifted_pair(suffix, prefix, BLK, step * k) for k in (1, 2, 3)]
        suffix = jnp.concatenate([pair[0] for pair in got] + [suffix], axis=0)
        prefix = jnp.concatenate([pair[1] for pair in got] + [prefix], axis=0)
        distances = [d + step * k for k in (1, 2, 3) for d in distances] + distances
        step *= 4
    late_suffix, got_prefix = shifted_pair(own_kv, prefix, BLK, reach)
    late_prefix = jnp.concatenate(
        [got_prefix]
        + [shifted(prefix, BLK, distance) for distance in range(2 * reach, blocks, reach)],
        axis=0,
    )
    count = suffix.shape[0]
    early_suffix = suffix.reshape(count * tok_rows, 2 * width)
    late_suffix = late_suffix.reshape(tok_rows, 2 * width)
    early_prefix = prefix.reshape(-1, 2 * width)
    late_prefix = late_prefix.reshape(-1, 2 * width)

    req_ends = jnp.cumsum(lengths)
    local_rows = jnp.arange(tok_rows, dtype=jnp.int32)
    query_pos = my_block * tok_rows + local_rows

    def owner_of(position):
        return jnp.sum((position[:, None] >= req_ends[None, :]).astype(jnp.int32), axis=1)

    query_owner = owner_of(query_pos)

    def visible_at(block_distances):
        block_of_key = my_block - jnp.repeat(jnp.array(block_distances, jnp.int32), tok_rows)
        key_pos = block_of_key * tok_rows + jnp.tile(local_rows, len(block_distances))
        key_owner = owner_of(key_pos)
        return (
            (key_owner[None, :] == query_owner[:, None])
            & (key_pos[None, :] <= query_pos[:, None])
            & (key_pos[None, :] >= 0)
        )

    early_visible = visible_at(distances)
    late_visible = visible_at([reach])

    heads_of_query = queries.reshape(tok_rows, kv_heads, heads_per_group, HEAD_SIZE)

    def scores_of(q, keys):
        return (
            jnp.einsum("qgd,kd->gqk", q, keys, preferred_element_type=jnp.float32) * score_scale
        )

    def weighted(weights, values):
        return jnp.einsum(
            "gqk,kd->gqd", weights.astype(jnp.bfloat16), values, preferred_element_type=jnp.float32
        )

    def piece(q, cols, vcols, prefix_rows, suffix_rows, visible):
        pre_scores = scores_of(q, prefix_rows[:, cols])
        suf_scores = jnp.where(visible[None], scores_of(q, suffix_rows[:, cols]), MASKED_SCORE)
        peak = jnp.maximum(jnp.max(pre_scores, axis=-1), jnp.max(suf_scores, axis=-1))
        pre_weights = jnp.exp(pre_scores - peak[..., None])
        suf_weights = jnp.where(visible[None], jnp.exp(suf_scores - peak[..., None]), 0.0)
        total = jnp.sum(pre_weights, axis=-1) + jnp.sum(suf_weights, axis=-1)
        summed = weighted(pre_weights, prefix_rows[:, vcols]) + weighted(
            suf_weights, suffix_rows[:, vcols]
        )
        return peak, total, summed

    def one_head(kv_head):
        cols = slice(kv_head * HEAD_SIZE, (kv_head + 1) * HEAD_SIZE)
        vcols = slice(width + kv_head * HEAD_SIZE, width + (kv_head + 1) * HEAD_SIZE)
        q = heads_of_query[:, kv_head]
        first_peak, first_total, first_sum = piece(
            q, cols, vcols, early_prefix, early_suffix, early_visible
        )
        late_peak, late_total, late_sum = piece(
            q, cols, vcols, late_prefix, late_suffix, late_visible
        )
        peak = jnp.maximum(first_peak, late_peak)
        first_scale = jnp.exp(first_peak - peak)
        late_scale = jnp.exp(late_peak - peak)
        total = first_total * first_scale + late_total * late_scale
        summed = first_sum * first_scale[..., None] + late_sum * late_scale[..., None]
        return summed / total[..., None]

    attended = jnp.stack([one_head(h) for h in range(kv_heads)])
    attn = (
        jnp.transpose(attended, (2, 0, 1, 3))
        .reshape(tok_rows, q_heads * HEAD_SIZE)
        .astype(jnp.bfloat16)
    )
    swap = [(0, 1), (1, 0)]
    core = lax.axis_index("core")
    both = jnp.concatenate((attn, lax.ppermute(attn, "core", swap)), axis=0)
    across = dict(BLK_PARTS)[BLK[1]]
    from_behind = [out_weight] + [
        lax.ppermute(out_weight, BLK[1], [((i - k) % across, i) for i in range(across)])
        for k in range(1, across)
    ]
    in_order = jnp.roll(jnp.stack(from_behind[::-1]), lax.axis_index(BLK[1]) + 1, axis=0)
    row = jnp.moveaxis(in_order, 0, 1)
    partner = lax.ppermute(row, BLK[2], swap)
    pair = jnp.where(
        lax.axis_index(BLK[2]) == 0,
        jnp.stack((row, partner), axis=2),
        jnp.stack((partner, row), axis=2),
    )
    weight = lax.all_gather(pair.reshape(out_weight.shape[0], -1), BLK[0], axis=1, tiled=True)
    product = jnp.dot(both, weight, preferred_element_type=jnp.float32)
    reduced = lax.psum_scatter(product.astype(jnp.bfloat16), "mp", scatter_dimension=1, tiled=True)
    other = lax.ppermute(reduced, "core", swap)[tok_rows:]
    mine = reduced[:tok_rows]
    per_block = out_weight.shape[1]
    mine = mine.reshape(tok_rows, -1, per_block)
    other = other.reshape(tok_rows, -1, per_block)
    even = jnp.where(core == 0, mine, other)
    odd = jnp.where(core == 0, other, mine)
    return jnp.stack((even, odd), axis=2).reshape(tok_rows, -1)


def solution(mesh):
    sizes = tuple(size for _, size in BLK_PARTS)
    split = jax.sharding.Mesh(
        mesh.devices.reshape(sizes + (mesh.shape["mp"],)), BLK + ("mp",)
    )
    placed = (
        P(BLK, "mp"),
        P(BLK, "mp"),
        P(BLK, "mp"),
        P(BLK, "mp"),
        P(BLK, "mp"),
        P("mp", BLK),
        P(),
    )
    return jax.shard_map(
        per_device, mesh=split, in_specs=placed, out_specs=P(BLK, "mp"), check_vma=False
    )
```
